32 devices in a mesh: row: 4 (over y, x), col: 8 (over z, core).
Axes of the slice: x: 2, y: 2, z: 4, core: 2. Of those that a mesh axis runs over, the one named last changes fastest.
Arguments:
- density: float32 [2048, 2048], P('row', 'col'), as said below
- pattern: int32 [16, 16], replicated, may hold values from 0 to 1, as said below
Outputs:
- purified: float32 [2048, 2048], P('row', 'col')
The draws below stay inside these ranges and needn't reach their ends.
Inputs may be any that keep to these rules, and one draw needn't show every extreme that they name: density is symmetric and zero outside the blocks that pattern allows. pattern is symmetric with ones on its diagonal, and every block row holds exactly 7 ones.
All inputs are finite; a program needn't handle non-finite values.
Results may differ from the reference program's by a relative error of at most 0.0061.
Values may be sent and summed in bfloat16 or wider, within the bound.
No kernel may reach another device: no remote copies, remote signals or barrier semaphores. Data moves between devices by JAX's collectives and lax.ppermute only.
A program may use at most 64 MiB of HBM per device.

```python
import math
import jax
import jax.numpy as jnp

BS = 128
WB = 3
STEPS = 2
NB = 16
ORDER = 2048


def cycle_blocks(key):
    placing = jax.random.permutation(jax.random.fold_in(key, 7), NB).astype(jnp.int32)
    distance = jnp.abs(placing[:, None] - placing[None, :])
    beside_all = jnp.minimum(distance, NB - distance)
    return (beside_all <= WB).astype(jnp.int32)


def draw_pattern(key, part):
    return cycle_blocks(key)


def draw_density(key, part):
    allowed = cycle_blocks(key)
    mask = jnp.repeat(jnp.repeat(allowed, BS, axis=0), BS, axis=1).astype(jnp.float32)
    first, second = jax.random.split(jax.random.fold_in(key, 11))
    values = jax.random.normal(first, (ORDER, ORDER), jnp.float32)
    spread = 0.3 / (math.sqrt(2.0) * math.sqrt((2 * WB + 1) * BS))
    upper = (values + values.T) * spread
    diagonal = 0.5 + 0.3 * jax.random.uniform(second, (ORDER,), jnp.float32, -1.0, 1.0)
    return mask * (upper + jnp.diag(diagonal))


def setup_inputs(seed: int = 0) -> dict:
    arg_keys = jax.random.split(jax.random.key(seed), 3)
    density = draw_density(jax.random.fold_in(arg_keys[2], 71), 0)
    pattern = draw_pattern(jax.random.fold_in(arg_keys[2], 71), 0)
    return dict(density=density, pattern=pattern)


def expand(pattern):
    count = pattern.shape[0]
    index = jnp.arange(count, dtype=jnp.int32)
    eye = (index[:, None] == index[None, :]).astype(jnp.int32)
    allowed = jnp.maximum(jnp.maximum(pattern, pattern.T), eye)
    return jnp.repeat(jnp.repeat(allowed, BS, axis=0), BS, axis=1).astype(jnp.float32)


def reference(density, pattern):
    mask = expand(pattern)
    current = mask * density
    for step in range(STEPS):
        xb = current.astype(jnp.bfloat16)
        square = mask * jnp.dot(xb, xb, preferred_element_type=jnp.float32)
        qb = square.astype(jnp.bfloat16)
        jordan = jnp.dot(qb, xb, preferred_element_type=jnp.float32) + jnp.dot(xb, qb, preferred_element_type=jnp.float32)
        current = mask * (3.0 * square - jordan)
    return current
```

```python
import jax
import jax.numpy as jnp
from jax import lax
from jax.sharding import PartitionSpec as P

BS = 128
STEPS = 2


def allowed_blocks(pattern):
    count = pattern.shape[0]
    index = lax.iota(jnp.int32, count)
    eye = (index[:, None] == index[None, :]).astype(jnp.int32)
    return jnp.maximum(jnp.maximum(pattern, pattern.T), eye)


def apply_mask(values, blocks):
    row_blocks, col_blocks = blocks.shape
    shaped = values.reshape(row_blocks, BS, col_blocks, BS) * blocks[:, None, :, None]
    return shaped.reshape(row_blocks * BS, col_blocks * BS)


def xor_permute(x, axis, size, s):
    return lax.ppermute(x, axis, perm=[(i, i ^ s) for i in range(size)])


def exchange(xb, n_row, n_col):
    col_pieces = [xb] + [xor_permute(xb, "row", n_row, t) for t in range(1, n_row)]
    chips = n_col // 2
    same_core = [xb] + [xor_permute(xb, "col", n_col, 2 * s) for s in range(1, chips)]
    partner_own = xor_permute(xb, "col", n_col, 1)
    relayed = xor_permute(jnp.stack(same_core[1:]), "col", n_col, 1)
    row_pieces = []
    for s in range(chips):
        row_pieces.append(same_core[s])
        row_pieces.append(partner_own if s == 0 else relayed[s - 1])
    return jnp.stack(row_pieces), jnp.stack(col_pieces)


def ordered_k_blocks(col_pieces, me_row, me_col, n_col):
    n_row, rows, cols = col_pieces.shape
    per = rows // cols
    split = col_pieces.reshape(n_row * per, cols, cols)
    s = lax.iota(jnp.int32, n_col)
    owner = jnp.bitwise_xor(s, me_col)
    index = jnp.bitwise_xor(owner // per, me_row) * per + owner % per
    return jnp.take(split, index, axis=0)


def contract(row_pieces, k_blocks):
    return jnp.einsum("sik,skj->ij", row_pieces, k_blocks, preferred_element_type=jnp.float32)


def on_device(density, pattern):
    rows, cols = density.shape
    row_blocks = rows // BS
    col_blocks = cols // BS
    n_row = lax.axis_size("row")
    n_col = lax.axis_size("col")
    me_row = lax.axis_index("row")
    me_col = lax.axis_index("col")
    allowed = allowed_blocks(pattern)
    blocks = lax.dynamic_slice(
        allowed, (me_row * row_blocks, me_col * col_blocks), (row_blocks, col_blocks)
    ).astype(jnp.float32)
    current = apply_mask(density, blocks)
    for step in range(STEPS):
        xb = current.astype(jnp.bfloat16)
        x_row, x_col = exchange(xb, n_row, n_col)
        x_k = ordered_k_blocks(x_col, me_row, me_col, n_col)
        square = apply_mask(contract(x_row, x_k), blocks)
        qb = square.astype(jnp.bfloat16)
        q_row, q_col = exchange(qb, n_row, n_col)
        q_k = ordered_k_blocks(q_col, me_row, me_col, n_col)
        jordan = contract(q_row, x_k) + contract(x_row, q_k)
        current = apply_mask(3.0 * square - jordan, blocks)
    return current


def solution(mesh):
    placed = (P("row", "col"), P())
    return jax.shard_map(
        on_device, mesh=mesh, in_specs=placed, out_specs=P("row", "col"), check_vma=False
    )
```

```python
import jax
import jax.numpy as jnp
from jax import lax
from jax.sharding import PartitionSpec as P

BS = 128
STEPS = 2


def allowed_blocks(pattern):
    count = pattern.shape[0]
    index = lax.iota(jnp.int32, count)
    eye = (index[:, None] == index[None, :]).astype(jnp.int32)
    return jnp.maximum(jnp.maximum(pattern, pattern.T), eye)


def apply_mask(values, blocks):
    row_blocks, col_blocks = blocks.shape
    shaped = values.reshape(row_blocks, BS, col_blocks, BS) * blocks[:, None, :, None]
    return shaped.reshape(row_blocks * BS, col_blocks * BS)


def xor_permute(x, axis, size, s):
    return lax.ppermute(x, axis, perm=[(i, i ^ s) for i in range(size)])


def exchange(xb, n_row, n_col):
    col_pieces = [xb] + [xor_permute(xb, "row", n_row, t) for t in range(1, n_row)]
    chips = n_col // 2
    same_core = [xb] + [xor_permute(xb, "col", n_col, 2 * s) for s in range(1, chips)]
    partner_own = xor_permute(xb, "col", n_col, 1)
    relayed = xor_permute(jnp.stack(same_core[1:]), "col", n_col, 1)
    row_pieces = []
    for s in range(chips):
        row_pieces.append(same_core[s])
        row_pieces.append(partner_own if s == 0 else relayed[s - 1])
    return row_pieces, jnp.stack(col_pieces)


def ordered_k_blocks(col_pieces, me_row, me_col, n_col):
    n_row, rows, cols = col_pieces.shape
    per = rows // cols
    split = col_pieces.reshape(n_row * per, cols, cols)
    s = lax.iota(jnp.int32, n_col)
    owner = jnp.bitwise_xor(s, me_col)
    index = jnp.bitwise_xor(owner // per, me_row) * per + owner % per
    return jnp.take(split, index, axis=0)


def contract(row_pieces, k_blocks):
    total = None
    for s, piece in enumerate(row_pieces):
        part = jnp.dot(piece, k_blocks[s], preferred_element_type=jnp.float32)
        total = part if total is None else total + part
    return total


def on_device(density, pattern):
    rows, cols = density.shape
    row_blocks = rows // BS
    col_blocks = cols // BS
    n_row = lax.axis_size("row")
    n_col = lax.axis_size("col")
    me_row = lax.axis_index("row")
    me_col = lax.axis_index("col")
    allowed = allowed_blocks(pattern)
    blocks = lax.dynamic_slice(
        allowed, (me_row * row_blocks, me_col * col_blocks), (row_blocks, col_blocks)
    ).astype(jnp.float32)
    current = apply_mask(density, blocks)
    for step in range(STEPS):
        xb = current.astype(jnp.bfloat16)
        x_row, x_col = exchange(xb, n_row, n_col)
        x_k = ordered_k_blocks(x_col, me_row, me_col, n_col)
        square = apply_mask(contract(x_row, x_k), blocks)
        qb = square.astype(jnp.bfloat16)
        q_row, q_col = exchange(qb, n_row, n_col)
        q_k = ordered_k_blocks(q_col, me_row, me_col, n_col)
        jordan = contract(q_row, x_k) + contract(x_row, q_k)
        current = apply_mask(3.0 * square - jordan, blocks)
    return current


def solution(mesh):
    placed = (P("row", "col"), P())
    return jax.shard_map(
        on_device, mesh=mesh, in_specs=placed, out_specs=P("row", "col"), check_vma=False
    )
```

```python
import functools

import jax
import jax.numpy as jnp
from jax import lax
from jax.experimental import pallas as pl
from jax.experimental.pallas import tpu as pltpu
from jax.sharding import PartitionSpec as P

BS = 128
STEPS = 2


def allowed_blocks(pattern):
    count = pattern.shape[0]
    index = lax.iota(jnp.int32, count)
    eye = (index[:, None] == index[None, :]).astype(jnp.int32)
    return jnp.maximum(jnp.maximum(pattern, pattern.T), eye)


def apply_mask(values, blocks):
    row_blocks, col_blocks = blocks.shape
    shaped = values.reshape(row_blocks, BS, col_blocks, BS) * blocks[:, None, :, None]
    return shaped.reshape(row_blocks * BS, col_blocks * BS)


def xor_permute(x, axis, size, s):
    return lax.ppermute(x, axis, perm=[(i, i ^ s) for i in range(size)])


def exchange(xb, n_row, n_col):
    col_pieces = [xb] + [xor_permute(xb, "row", n_row, t) for t in range(1, n_row)]
    chips = n_col // 2
    same_core = [xb] + [xor_permute(xb, "col", n_col, 2 * s) for s in range(1, chips)]
    partner_own = xor_permute(xb, "col", n_col, 1)
    relayed = xor_permute(jnp.stack(same_core[1:]), "col", n_col, 1)
    row_pieces = []
    for s in range(chips):
        row_pieces.append(same_core[s])
        row_pieces.append(partner_own if s == 0 else relayed[s - 1])
    return row_pieces, jnp.stack(col_pieces)


def ordered_k_blocks(col_pieces, me_row, me_col, n_col):
    n_row, rows, cols = col_pieces.shape
    per = rows // cols
    split = col_pieces.reshape(n_row * per, cols, cols)
    s = lax.iota(jnp.int32, n_col)
    owner = jnp.bitwise_xor(s, me_col)
    index = jnp.bitwise_xor(owner // per, me_row) * per + owner % per
    return jnp.take(split, index, axis=0)


def square_kernel(n, *refs):
    pieces = refs[:n]
    k_ref, mask_ref, square_ref, qb_ref = refs[n:]
    acc = jnp.dot(pieces[0][...], k_ref[0], preferred_element_type=jnp.float32)
    for s in range(1, n):
        acc = acc + jnp.dot(pieces[s][...], k_ref[s], preferred_element_type=jnp.float32)
    square = acc * mask_ref[...]
    square_ref[...] = square
    qb_ref[...] = square.astype(jnp.bfloat16)


def jordan_kernel(n, *refs):
    q_pieces = refs[:n]
    x_pieces = refs[n:2 * n]
    xk_ref, qk_ref, square_ref, mask_ref, current_ref, xb_ref = refs[2 * n:]
    acc = jnp.dot(q_pieces[0][...], xk_ref[0], preferred_element_type=jnp.float32)
    acc = acc + jnp.dot(x_pieces[0][...], qk_ref[0], preferred_element_type=jnp.float32)
    for s in range(1, n):
        acc = acc + jnp.dot(q_pieces[s][...], xk_ref[s], preferred_element_type=jnp.float32)
        acc = acc + jnp.dot(x_pieces[s][...], qk_ref[s], preferred_element_type=jnp.float32)
    current = mask_ref[...] * (3.0 * square_ref[...] - acc)
    current_ref[...] = current
    xb_ref[...] = current.astype(jnp.bfloat16)


def vmem_spec():
    return pl.BlockSpec(memory_space=pltpu.VMEM)


def square_call(pieces, k_blocks, mask):
    n = len(pieces)
    rows, cols = mask.shape
    out = (
        jax.ShapeDtypeStruct((rows, cols), jnp.float32),
        jax.ShapeDtypeStruct((rows, cols), jnp.bfloat16),
    )
    cost = pl.CostEstimate(
        flops=2 * rows * cols * cols * n,
        transcendentals=0,
        bytes_accessed=2 * rows * cols * n + 2 * cols * cols * n + 10 * rows * cols,
    )
    return pl.pallas_call(
        functools.partial(square_kernel, n),
        out_shape=out,
        in_specs=[vmem_spec()] * (n + 2),
        out_specs=(vmem_spec(), vmem_spec()),
        cost_estimate=cost,
        name="square_panels",
    )(*pieces, k_blocks, mask)


def jordan_call(q_pieces, x_pieces, xk, qk, square, mask):
    n = len(q_pieces)
    rows, cols = mask.shape
    out = (
        jax.ShapeDtypeStruct((rows, cols), jnp.float32),
        jax.ShapeDtypeStruct((rows, cols), jnp.bfloat16),
    )
    cost = pl.CostEstimate(
        flops=4 * rows * cols * cols * n,
        transcendentals=0,
        bytes_accessed=4 * rows * cols * n + 4 * cols * cols * n + 14 * rows * cols,
    )
    return pl.pallas_call(
        functools.partial(jordan_kernel, n),
        out_shape=out,
        in_specs=[vmem_spec()] * (2 * n + 4),
        out_specs=(vmem_spec(), vmem_spec()),
        cost_estimate=cost,
        name="jordan_panels",
    )(*q_pieces, *x_pieces, xk, qk, square, mask)


def on_device(density, pattern):
    rows, cols = density.shape
    row_blocks = rows // BS
    col_blocks = cols // BS
    n_row = lax.axis_size("row")
    n_col = lax.axis_size("col")
    me_row = lax.axis_index("row")
    me_col = lax.axis_index("col")
    allowed = allowed_blocks(pattern)
    blocks = lax.dynamic_slice(
        allowed, (me_row * row_blocks, me_col * col_blocks), (row_blocks, col_blocks)
    ).astype(jnp.float32)
    mask = apply_mask(jnp.ones((rows, cols), jnp.float32), blocks)
    current = mask * density
    xb = current.astype(jnp.bfloat16)
    for step in range(STEPS):
        x_row, x_col = exchange(xb, n_row, n_col)
        x_k = ordered_k_blocks(x_col, me_row, me_col, n_col)
        square, qb = square_call(x_row, x_k, mask)
        q_row, q_col = exchange(qb, n_row, n_col)
        q_k = ordered_k_blocks(q_col, me_row, me_col, n_col)
        current, xb = jordan_call(q_row, x_row, x_k, q_k, square, mask)
    return current


def solution(mesh):
    placed = (P("row", "col"), P())
    return jax.shard_map(
        on_device, mesh=mesh, in_specs=placed, out_specs=P("row", "col"), check_vma=False
    )
```

```python
import jax
import jax.numpy as jnp
from jax import lax
from jax.sharding import PartitionSpec as P

BS = 128
STEPS = 2


def allowed_blocks(pattern):
    count = pattern.shape[0]
    index = lax.iota(jnp.int32, count)
    eye = (index[:, None] == index[None, :]).astype(jnp.int32)
    return jnp.maximum(jnp.maximum(pattern, pattern.T), eye)


def apply_mask(values, blocks):
    row_blocks, col_blocks = blocks.shape
    shaped = values.reshape(row_blocks, BS, col_blocks, BS) * blocks[:, None, :, None]
    return shaped.reshape(row_blocks * BS, col_blocks * BS)


def xor_permute(x, axis, size, s):
    return lax.ppermute(x, axis, perm=[(i, i ^ s) for i in range(size)])


def exchange(xb, n_row, n_col):
    col_pieces = [xb] + [xor_permute(xb, "row", n_row, t) for t in range(1, n_row)]
    chips = n_col // 2
    same = {0: xb}
    for s in [1] + list(range(2, chips, 2)):
        same[s] = xor_permute(xb, "col", n_col, 2 * s)
    partner_own = xor_permute(xb, "col", n_col, 1)
    first = sorted(s for s in same if s != 0)
    relay_first = xor_permute(jnp.stack([same[s] for s in first]), "col", n_col, 1)
    other = {0: partner_own}
    for i, s in enumerate(first):
        other[s] = relay_first[i]
    forward = list(range(2, chips, 2))
    if forward:
        sent = xor_permute(jnp.stack([same[s] for s in forward]), "col", n_col, 2)
        relay_sent = xor_permute(sent, "col", n_col, 1)
        for i, s in enumerate(forward):
            same[s ^ 1] = sent[i]
            other[s ^ 1] = relay_sent[i]
    row_pieces = []
    for s in range(chips):
        row_pieces.append(same[s])
        row_pieces.append(other[s])
    return row_pieces, jnp.stack(col_pieces)


def ordered_k_blocks(col_pieces, me_row, me_col, n_col):
    n_row, rows, cols = col_pieces.shape
    per = rows // cols
    split = col_pieces.reshape(n_row * per, cols, cols)
    s = lax.iota(jnp.int32, n_col)
    owner = jnp.bitwise_xor(s, me_col)
    index = jnp.bitwise_xor(owner // per, me_row) * per + owner % per
    return jnp.take(split, index, axis=0)


def contract(row_pieces, k_blocks):
    total = None
    for s, piece in enumerate(row_pieces):
        part = jnp.dot(piece, k_blocks[s], preferred_element_type=jnp.float32)
        total = part if total is None else total + part
    return total


def on_device(density, pattern):
    rows, cols = density.shape
    row_blocks = rows // BS
    col_blocks = cols // BS
    n_row = lax.axis_size("row")
    n_col = lax.axis_size("col")
    me_row = lax.axis_index("row")
    me_col = lax.axis_index("col")
    allowed = allowed_blocks(pattern)
    blocks = lax.dynamic_slice(
        allowed, (me_row * row_blocks, me_col * col_blocks), (row_blocks, col_blocks)
    ).astype(jnp.float32)
    current = apply_mask(density, blocks)
    for step in range(STEPS):
        xb = current.astype(jnp.bfloat16)
        x_row, x_col = exchange(xb, n_row, n_col)
        x_k = ordered_k_blocks(x_col, me_row, me_col, n_col)
        square = apply_mask(contract(x_row, x_k), blocks)
        qb = square.astype(jnp.bfloat16)
        q_row, q_col = exchange(qb, n_row, n_col)
        q_k = ordered_k_blocks(q_col, me_row, me_col, n_col)
        jordan = contract(q_row, x_k) + contract(x_row, q_k)
        current = apply_mask(3.0 * square - jordan, blocks)
    return current


def solution(mesh):
    placed = (P("row", "col"), P())
    return jax.shard_map(
        on_device, mesh=mesh, in_specs=placed, out_specs=P("row", "col"), check_vma=False
    )
```

```python
import jax
import jax.numpy as jnp
from jax import lax
from jax.sharding import PartitionSpec as P

BS = 128
STEPS = 2


def allowed_blocks(pattern):
    count = pattern.shape[0]
    index = lax.iota(jnp.int32, count)
    eye = (index[:, None] == index[None, :]).astype(jnp.int32)
    return jnp.maximum(jnp.maximum(pattern, pattern.T), eye)


def apply_mask(values, blocks):
    row_blocks, col_blocks = blocks.shape
    shaped = values.reshape(row_blocks, BS, col_blocks, BS) * blocks[:, None, :, None]
    return shaped.reshape(row_blocks * BS, col_blocks * BS)


def xor_permute(x, axis, size, s):
    return lax.ppermute(x, axis, perm=[(i, i ^ s) for i in range(size)])


def exchange(xb, n_row, n_col):
    col_pieces = lax.all_to_all(
        jnp.broadcast_to(xb[None], (n_row,) + xb.shape), "row", 0, 0, tiled=True
    )
    chips = n_col // 2
    same = {0: xb}
    for s in [1] + list(range(2, chips, 2)):
        same[s] = xor_permute(xb, "col", n_col, 2 * s)
    partner_own = xor_permute(xb, "col", n_col, 1)
    first = sorted(s for s in same if s != 0)
    relay_first = xor_permute(jnp.stack([same[s] for s in first]), "col", n_col, 1)
    other = {0: partner_own}
    for i, s in enumerate(first):
        other[s] = relay_first[i]
    forward = list(range(2, chips, 2))
    if forward:
        sent = xor_permute(jnp.stack([same[s] for s in forward]), "col", n_col, 2)
        relay_sent = xor_permute(sent, "col", n_col, 1)
        for i, s in enumerate(forward):
            same[s ^ 1] = sent[i]
            other[s ^ 1] = relay_sent[i]
    row_pieces = []
    for s in range(chips):
        row_pieces.append(same[s])
        row_pieces.append(other[s])
    return row_pieces, col_pieces


def ordered_k_blocks(col_pieces, me_row, me_col, n_col):
    n_row, rows, cols = col_pieces.shape
    split = col_pieces.reshape(n_row * rows // cols, cols, cols)
    s = lax.iota(jnp.int32, n_col)
    owner = jnp.bitwise_xor(s, me_col)
    index = owner
    return jnp.take(split, index, axis=0)


def contract(row_pieces, k_blocks):
    total = None
    for s, piece in enumerate(row_pieces):
        part = jnp.dot(piece, k_blocks[s], preferred_element_type=jnp.float32)
        total = part if total is None else total + part
    return total


def on_device(density, pattern):
    rows, cols = density.shape
    row_blocks = rows // BS
    col_blocks = cols // BS
    n_row = lax.axis_size("row")
    n_col = lax.axis_size("col")
    me_row = lax.axis_index("row")
    me_col = lax.axis_index("col")
    allowed = allowed_blocks(pattern)
    blocks = lax.dynamic_slice(
        allowed, (me_row * row_blocks, me_col * col_blocks), (row_blocks, col_blocks)
    ).astype(jnp.float32)
    current = apply_mask(density, blocks)
    for step in range(STEPS):
        xb = current.astype(jnp.bfloat16)
        x_row, x_col = exchange(xb, n_row, n_col)
        x_k = ordered_k_blocks(x_col, me_row, me_col, n_col)
        square = apply_mask(contract(x_row, x_k), blocks)
        qb = square.astype(jnp.bfloat16)
        q_row, q_col = exchange(qb, n_row, n_col)
        q_k = ordered_k_blocks(q_col, me_row, me_col, n_col)
        jordan = contract(q_row, x_k) + contract(x_row, q_k)
        current = apply_mask(3.0 * square - jordan, blocks)
    return current


def solution(mesh):
    placed = (P("row", "col"), P())
    return jax.shard_map(
        on_device, mesh=mesh, in_specs=placed, out_specs=P("row", "col"), check_vma=False
    )
```

```python
import jax
import jax.numpy as jnp
from jax import lax
from jax.sharding import PartitionSpec as P

BS = 128
STEPS = 2


def allowed_blocks(pattern):
    count = pattern.shape[0]
    index = lax.iota(jnp.int32, count)
    eye = (index[:, None] == index[None, :]).astype(jnp.int32)
    return jnp.maximum(jnp.maximum(pattern, pattern.T), eye)


def apply_mask(values, blocks):
    row_blocks, col_blocks = blocks.shape
    shaped = values.reshape(row_blocks, BS, col_blocks, BS) * blocks[:, None, :, None]
    return shaped.reshape(row_blocks * BS, col_blocks * BS)


def xor_permute(x, axis, size, s):
    return lax.ppermute(x, axis, perm=[(i, i ^ s) for i in range(size)])


def exchange(xb, n_row, n_col):
    chips = n_col // 2
    same = {0: xb}
    for s in sorted(range(2, chips, 2), reverse=True) + [1]:
        same[s] = xor_permute(xb, "col", n_col, 2 * s)
    col_pieces = [xb] + [xor_permute(xb, "row", n_row, t) for t in range(1, n_row)]
    first = sorted(same)
    relay_first = xor_permute(jnp.stack([same[s] for s in first]), "col", n_col, 1)
    other = {}
    for i, s in enumerate(first):
        other[s] = relay_first[i]
    forward = list(range(2, chips, 2))
    if forward:
        sent = xor_permute(jnp.stack([same[s] for s in forward]), "col", n_col, 2)
        relay_sent = xor_permute(sent, "col", n_col, 1)
        for i, s in enumerate(forward):
            same[s ^ 1] = sent[i]
            other[s ^ 1] = relay_sent[i]
    row_pieces = []
    for s in range(chips):
        row_pieces.append(same[s])
        row_pieces.append(other[s])
    return row_pieces, jnp.stack(col_pieces)


def ordered_k_blocks(col_pieces, me_row, me_col, n_col):
    n_row, rows, cols = col_pieces.shape
    per = rows // cols
    split = col_pieces.reshape(n_row * per, cols, cols)
    s = lax.iota(jnp.int32, n_col)
    owner = jnp.bitwise_xor(s, me_col)
    index = jnp.bitwise_xor(owner // per, me_row) * per + owner % per
    return jnp.take(split, index, axis=0)


def contract(row_pieces, k_blocks):
    total = None
    for s, piece in enumerate(row_pieces):
        part = jnp.dot(piece, k_blocks[s], preferred_element_type=jnp.float32)
        total = part if total is None else total + part
    return total


def on_device(density, pattern):
    rows, cols = density.shape
    row_blocks = rows // BS
    col_blocks = cols // BS
    n_row = lax.axis_size("row")
    n_col = lax.axis_size("col")
    me_row = lax.axis_index("row")
    me_col = lax.axis_index("col")
    allowed = allowed_blocks(pattern)
    blocks = lax.dynamic_slice(
        allowed, (me_row * row_blocks, me_col * col_blocks), (row_blocks, col_blocks)
    ).astype(jnp.float32)
    current = apply_mask(density, blocks)
    for step in range(STEPS):
        xb = current.astype(jnp.bfloat16)
        x_row, x_col = exchange(xb, n_row, n_col)
        x_k = ordered_k_blocks(x_col, me_row, me_col, n_col)
        square = apply_mask(contract(x_row, x_k), blocks)
        qb = square.astype(jnp.bfloat16)
        q_row, q_col = exchange(qb, n_row, n_col)
        q_k = ordered_k_blocks(q_col, me_row, me_col, n_col)
        jordan = contract(q_row, x_k) + contract(x_row, q_k)
        current = apply_mask(3.0 * square - jordan, blocks)
    return current


def solution(mesh):
    placed = (P("row", "col"), P())
    return jax.shard_map(
        on_device, mesh=mesh, in_specs=placed, out_specs=P("row", "col"), check_vma=False
    )
```

```python
import jax
import jax.numpy as jnp
from jax import lax
from jax.sharding import PartitionSpec as P

BS = 128
STEPS = 2


def allowed_blocks(pattern):
    count = pattern.shape[0]
    index = lax.iota(jnp.int32, count)
    eye = (index[:, None] == index[None, :]).astype(jnp.int32)
    return jnp.maximum(jnp.maximum(pattern, pattern.T), eye)


def apply_mask(values, blocks):
    row_blocks, col_blocks = blocks.shape
    shaped = values.reshape(row_blocks, BS, col_blocks, BS) * blocks[:, None, :, None]
    return shaped.reshape(row_blocks * BS, col_blocks * BS)


def xor_permute(x, axis, size, s):
    return lax.ppermute(x, axis, perm=[(i, i ^ s) for i in range(size)])


def exchange(xb, n_row, n_col):
    chips = n_col // 2
    half = xb.shape[1] // 2
    parts = (xb[:, :half], xb[:, half:])
    forward = list(range(2, chips, 2))
    same = {0: xb}
    for s in sorted(forward, reverse=True):
        same[s] = tuple(xor_permute(p, "col", n_col, 2 * s) for p in parts)
    same[1] = xor_permute(xb, "col", n_col, 2)
    col_pieces = [xb] + [xor_permute(xb, "row", n_row, t) for t in range(1, n_row)]
    relay_first = xor_permute(jnp.stack([xb, same[1]]), "col", n_col, 1)
    other = {0: relay_first[0], 1: relay_first[1]}
    if forward:
        relay_halves = xor_permute(
            jnp.stack([p for s in forward for p in same[s]]), "col", n_col, 1
        )
        sent = [
            xor_permute(jnp.stack([same[s][h] for s in forward]), "col", n_col, 2) for h in (0, 1)
        ]
        relay_sent = xor_permute(jnp.stack(sent), "col", n_col, 1)
        for i, s in enumerate(forward):
            other[s] = (relay_halves[2 * i], relay_halves[2 * i + 1])
            same[s ^ 1] = (sent[0][i], sent[1][i])
            other[s ^ 1] = (relay_sent[0, i], relay_sent[1, i])
    row_pieces = []
    for s in range(chips):
        row_pieces.append(same[s])
        row_pieces.append(other[s])
    return row_pieces, jnp.stack(col_pieces)


def ordered_k_blocks(col_pieces, me_row, me_col, n_col):
    n_row, rows, cols = col_pieces.shape
    per = rows // cols
    split = col_pieces.reshape(n_row * per, cols, cols)
    s = lax.iota(jnp.int32, n_col)
    owner = jnp.bitwise_xor(s, me_col)
    index = jnp.bitwise_xor(owner // per, me_row) * per + owner % per
    return jnp.take(split, index, axis=0)


def contract(row_pieces, k_blocks):
    total = None
    for s, piece in enumerate(row_pieces):
        if isinstance(piece, tuple):
            half = piece[0].shape[1]
            parts = [
                jnp.dot(piece[0], k_blocks[s, :half], preferred_element_type=jnp.float32),
                jnp.dot(piece[1], k_blocks[s, half:], preferred_element_type=jnp.float32),
            ]
        else:
            parts = [jnp.dot(piece, k_blocks[s], preferred_element_type=jnp.float32)]
        for part in parts:
            total = part if total is None else total + part
    return total


def on_device(density, pattern):
    rows, cols = density.shape
    row_blocks = rows // BS
    col_blocks = cols // BS
    n_row = lax.axis_size("row")
    n_col = lax.axis_size("col")
    me_row = lax.axis_index("row")
    me_col = lax.axis_index("col")
    allowed = allowed_blocks(pattern)
    blocks = lax.dynamic_slice(
        allowed, (me_row * row_blocks, me_col * col_blocks), (row_blocks, col_blocks)
    ).astype(jnp.float32)
    current = apply_mask(density, blocks)
    for step in range(STEPS):
        xb = current.astype(jnp.bfloat16)
        x_row, x_col = exchange(xb, n_row, n_col)
        x_k = ordered_k_blocks(x_col, me_row, me_col, n_col)
        square = apply_mask(contract(x_row, x_k), blocks)
        qb = square.astype(jnp.bfloat16)
        q_row, q_col = exchange(qb, n_row, n_col)
        q_k = ordered_k_blocks(q_col, me_row, me_col, n_col)
        jordan = contract(q_row, x_k) + contract(x_row, q_k)
        current = apply_mask(3.0 * square - jordan, blocks)
    return current


def solution(mesh):
    placed = (P("row", "col"), P())
    return jax.shard_map(
        on_device, mesh=mesh, in_specs=placed, out_specs=P("row", "col"), check_vma=False
    )
```

```python
import jax
import jax.numpy as jnp
from jax import lax
from jax.sharding import PartitionSpec as P

BS = 128
STEPS = 2


def allowed_blocks(pattern):
    count = pattern.shape[0]
    index = lax.iota(jnp.int32, count)
    eye = (index[:, None] == index[None, :]).astype(jnp.int32)
    return jnp.maximum(jnp.maximum(pattern, pattern.T), eye)


def apply_mask(values, blocks):
    row_blocks, col_blocks = blocks.shape
    shaped = values.reshape(row_blocks, BS, col_blocks, BS) * blocks[:, None, :, None]
    return shaped.reshape(row_blocks * BS, col_blocks * BS)


def xor_permute(x, axis, size, s):
    return lax.ppermute(x, axis, perm=[(i, i ^ s) for i in range(size)])


def exchange(xb, n_row, n_col):
    chips = n_col // 2
    same = {0: xb}
    for s in sorted(range(2, chips, 2), reverse=True) + [1]:
        same[s] = xor_permute(xb, "col", n_col, 2 * s)
    col_pieces = [xb] + [xor_permute(xb, "row", n_row, t) for t in range(1, n_row)]
    first = sorted(same)
    relay_first = xor_permute(jnp.stack([same[s] for s in first]), "col", n_col, 1)
    other = {}
    for i, s in enumerate(first):
        other[s] = relay_first[i]
    forward = list(range(2, chips, 2))
    if forward:
        held = jnp.stack([same[s] for s in forward])
        sent = xor_permute(held, "col", n_col, 2)
        sent_other = xor_permute(held, "col", n_col, 3)
        for i, s in enumerate(forward):
            same[s ^ 1] = sent[i]
            other[s ^ 1] = sent_other[i]
    row_pieces = []
    for s in range(chips):
        row_pieces.append(same[s])
        row_pieces.append(other[s])
    return row_pieces, jnp.stack(col_pieces)


def ordered_k_blocks(col_pieces, me_row, me_col, n_col):
    n_row, rows, cols = col_pieces.shape
    per = rows // cols
    split = col_pieces.reshape(n_row * per, cols, cols)
    s = lax.iota(jnp.int32, n_col)
    owner = jnp.bitwise_xor(s, me_col)
    index = jnp.bitwise_xor(owner // per, me_row) * per + owner % per
    return jnp.take(split, index, axis=0)


def contract(row_pieces, k_blocks):
    total = None
    for s, piece in enumerate(row_pieces):
        part = jnp.dot(piece, k_blocks[s], preferred_element_type=jnp.float32)
        total = part if total is None else total + part
    return total


def on_device(density, pattern):
    rows, cols = density.shape
    row_blocks = rows // BS
    col_blocks = cols // BS
    n_row = lax.axis_size("row")
    n_col = lax.axis_size("col")
    me_row = lax.axis_index("row")
    me_col = lax.axis_index("col")
    allowed = allowed_blocks(pattern)
    blocks = lax.dynamic_slice(
        allowed, (me_row * row_blocks, me_col * col_blocks), (row_blocks, col_blocks)
    ).astype(jnp.float32)
    current = apply_mask(density, blocks)
    for step in range(STEPS):
        xb = current.astype(jnp.bfloat16)
        x_row, x_col = exchange(xb, n_row, n_col)
        x_k = ordered_k_blocks(x_col, me_row, me_col, n_col)
        square = apply_mask(contract(x_row, x_k), blocks)
        qb = square.astype(jnp.bfloat16)
        q_row, q_col = exchange(qb, n_row, n_col)
        q_k = ordered_k_blocks(q_col, me_row, me_col, n_col)
        jordan = contract(q_row, x_k) + contract(x_row, q_k)
        current = apply_mask(3.0 * square - jordan, blocks)
    return current


def solution(mesh):
    placed = (P("row", "col"), P())
    return jax.shard_map(
        on_device, mesh=mesh, in_specs=placed, out_specs=P("row", "col"), check_vma=False
    )
```

```python
import jax
import jax.numpy as jnp
from jax import lax
from jax.sharding import PartitionSpec as P

BS = 128
STEPS = 2


def allowed_blocks(pattern):
    count = pattern.shape[0]
    index = lax.iota(jnp.int32, count)
    eye = (index[:, None] == index[None, :]).astype(jnp.int32)
    return jnp.maximum(jnp.maximum(pattern, pattern.T), eye)


def apply_mask(values, blocks):
    row_blocks, col_blocks = blocks.shape
    shaped = values.reshape(row_blocks, BS, col_blocks, BS) * blocks[:, None, :, None]
    return shaped.reshape(row_blocks * BS, col_blocks * BS)


def xor_permute(x, axis, size, s):
    return lax.ppermute(x, axis, perm=[(i, i ^ s) for i in range(size)])


def exchange(xb, n_row, n_col):
    chips = n_col // 2
    same = {0: xb}
    for s in sorted(range(2, chips, 2), reverse=True) + [1]:
        same[s] = xor_permute(xb, "col", n_col, 2 * s)
    col_same = [xb] + [xor_permute(xb, "row", n_row, t) for t in range(1, n_row)]
    forward = list(range(2, chips, 2))
    if forward:
        sent = xor_permute(jnp.stack([same[s] for s in forward]), "col", n_col, 2)
        for i, s in enumerate(forward):
            same[s ^ 1] = sent[i]
    mine = jnp.stack(col_same)
    partner = xor_permute(mine, "col", n_col, 1)
    return [same[s] for s in range(chips)], mine, partner


def ordered_k_blocks(mine, partner, me_row, core, chip, chips):
    n_row, half, wide = mine.shape
    per = wide // half
    both = jnp.concatenate([mine, partner], axis=0)
    s = lax.iota(jnp.int32, chips)
    first = jnp.bitwise_xor(s, chip)[:, None] * per + lax.iota(jnp.int32, per)[None, :]
    index = jnp.bitwise_xor(first % 2, core) * n_row + jnp.bitwise_xor(first // 2, me_row)
    picked = jnp.take(both, index.reshape(-1), axis=0)
    return picked.reshape(chips, per * half, wide)


def contract(row_pieces, k_blocks):
    total = None
    for s, piece in enumerate(row_pieces):
        part = jnp.dot(piece, k_blocks[s], preferred_element_type=jnp.float32)
        total = part if total is None else total + part
    return total


def swap_halves(keep, give, core, n_col, axis):
    got = xor_permute(give, "col", n_col, 1)
    first = jnp.where(core == 0, keep, got)
    second = jnp.where(core == 0, got, keep)
    return jnp.concatenate([first, second], axis=axis)


def on_device(density, pattern):
    rows, cols = density.shape
    half = rows // 2
    wide = 2 * cols
    n_row = lax.axis_size("row")
    n_col = lax.axis_size("col")
    chips = n_col // 2
    me_row = lax.axis_index("row")
    me_col = lax.axis_index("col")
    core = me_col % 2
    chip = me_col // 2
    allowed = allowed_blocks(pattern)
    blocks = lax.dynamic_slice(
        allowed,
        ((me_row * rows + core * half) // BS, chip * wide // BS),
        (half // BS, wide // BS),
    ).astype(jnp.float32)
    rounded = density.astype(jnp.bfloat16)
    keep = lax.dynamic_slice_in_dim(rounded, core * half, half, axis=0)
    give = lax.dynamic_slice_in_dim(rounded, (1 - core) * half, half, axis=0)
    xb = apply_mask(swap_halves(keep, give, core, n_col, 1), blocks).astype(jnp.bfloat16)
    for step in range(STEPS):
        x_row, x_mine, x_partner = exchange(xb, n_row, n_col)
        x_k = ordered_k_blocks(x_mine, x_partner, me_row, core, chip, chips)
        square = apply_mask(contract(x_row, x_k), blocks)
        qb = square.astype(jnp.bfloat16)
        q_row, q_mine, q_partner = exchange(qb, n_row, n_col)
        q_k = ordered_k_blocks(q_mine, q_partner, me_row, core, chip, chips)
        jordan = contract(q_row, x_k) + contract(x_row, q_k)
        current = apply_mask(3.0 * square - jordan, blocks)
        xb = current.astype(jnp.bfloat16)
    keep = lax.dynamic_slice_in_dim(current, core * cols, cols, axis=1)
    give = lax.dynamic_slice_in_dim(current, (1 - core) * cols, cols, axis=1)
    return swap_halves(keep, give, core, n_col, 0)


def solution(mesh):
    placed = (P("row", "col"), P())
    return jax.shard_map(
        on_device, mesh=mesh, in_specs=placed, out_specs=P("row", "col"), check_vma=False
    )
```

```python
import jax
import jax.numpy as jnp
from jax import lax
from jax.sharding import PartitionSpec as P

BS = 128
STEPS = 2


def allowed_blocks(pattern):
    count = pattern.shape[0]
    index = lax.iota(jnp.int32, count)
    eye = (index[:, None] == index[None, :]).astype(jnp.int32)
    return jnp.maximum(jnp.maximum(pattern, pattern.T), eye)


def apply_mask(values, blocks):
    row_blocks, col_blocks = blocks.shape
    shaped = values.reshape(row_blocks, BS, col_blocks, BS) * blocks[:, None, :, None]
    return shaped.reshape(row_blocks * BS, col_blocks * BS)


def xor_permute(x, axis, size, s):
    return lax.ppermute(x, axis, perm=[(i, i ^ s) for i in range(size)])


def exchange(xb, n_row, n_col):
    chips = n_col // 2
    half = xb.shape[1] // 2
    parts = (xb[:, :half], xb[:, half:])
    forward = list(range(2, chips, 2))
    same = {0: xb}
    for s in sorted(forward, reverse=True):
        same[s] = [xor_permute(parts[0], "col", n_col, 2 * s)]
    same[1] = xor_permute(xb, "col", n_col, 2)
    col_pieces = [xb] + [xor_permute(xb, "row", n_row, t) for t in range(1, n_row)]
    relay_first = xor_permute(jnp.stack([xb, same[1]]), "col", n_col, 1)
    other = {0: relay_first[0], 1: relay_first[1]}
    if forward:
        for s in sorted(forward, reverse=True):
            later, landed = lax.optimization_barrier((parts[1], same[s][0]))
            same[s] = [landed, xor_permute(later, "col", n_col, 2 * s)]
        sent = [
            xor_permute(jnp.stack([same[s][h] for s in forward]), "col", n_col, 2) for h in (0, 1)
        ]
        relay_halves = xor_permute(
            jnp.stack([same[s][h] for s in forward for h in (0, 1)]), "col", n_col, 1
        )
        relay_sent = xor_permute(jnp.stack(sent), "col", n_col, 1)
        for i, s in enumerate(forward):
            other[s] = (relay_halves[2 * i], relay_halves[2 * i + 1])
            same[s ^ 1] = (sent[0][i], sent[1][i])
            other[s ^ 1] = (relay_sent[0, i], relay_sent[1, i])
            same[s] = tuple(same[s])
    row_pieces = []
    for s in range(chips):
        row_pieces.append(same[s])
        row_pieces.append(other[s])
    return row_pieces, jnp.stack(col_pieces)


def ordered_k_blocks(col_pieces, me_row, me_col, n_col):
    n_row, rows, cols = col_pieces.shape
    per = rows // cols
    split = col_pieces.reshape(n_row * per, cols, cols)
    s = lax.iota(jnp.int32, n_col)
    owner = jnp.bitwise_xor(s, me_col)
    index = jnp.bitwise_xor(owner // per, me_row) * per + owner % per
    return jnp.take(split, index, axis=0)


def contract(row_pieces, k_blocks):
    total = None
    for s, piece in enumerate(row_pieces):
        if isinstance(piece, tuple):
            half = piece[0].shape[1]
            parts = [
                jnp.dot(piece[0], k_blocks[s, :half], preferred_element_type=jnp.float32),
                jnp.dot(piece[1], k_blocks[s, half:], preferred_element_type=jnp.float32),
            ]
        else:
            parts = [jnp.dot(piece, k_blocks[s], preferred_element_type=jnp.float32)]
        for part in parts:
            total = part if total is None else total + part
    return total


def on_device(density, pattern):
    rows, cols = density.shape
    row_blocks = rows // BS
    col_blocks = cols // BS
    n_row = lax.axis_size("row")
    n_col = lax.axis_size("col")
    me_row = lax.axis_index("row")
    me_col = lax.axis_index("col")
    allowed = allowed_blocks(pattern)
    blocks = lax.dynamic_slice(
        allowed, (me_row * row_blocks, me_col * col_blocks), (row_blocks, col_blocks)
    ).astype(jnp.float32)
    current = apply_mask(density, blocks)
    for step in range(STEPS):
        xb = current.astype(jnp.bfloat16)
        x_row, x_col = exchange(xb, n_row, n_col)
        x_k = ordered_k_blocks(x_col, me_row, me_col, n_col)
        square = apply_mask(contract(x_row, x_k), blocks)
        qb = square.astype(jnp.bfloat16)
        q_row, q_col = exchange(qb, n_row, n_col)
        q_k = ordered_k_blocks(q_col, me_row, me_col, n_col)
        jordan = contract(q_row, x_k) + contract(x_row, q_k)
        current = apply_mask(3.0 * square - jordan, blocks)
    return current


def solution(mesh):
    placed = (P("row", "col"), P())
    return jax.shard_map(
        on_device, mesh=mesh, in_specs=placed, out_specs=P("row", "col"), check_vma=False
    )
```

```python
import jax
import jax.numpy as jnp
from jax import lax
from jax.sharding import PartitionSpec as P

BS = 128
STEPS = 2


def allowed_blocks(pattern):
    count = pattern.shape[0]
    index = lax.iota(jnp.int32, count)
    eye = (index[:, None] == index[None, :]).astype(jnp.int32)
    return jnp.maximum(jnp.maximum(pattern, pattern.T), eye)


def apply_mask(values, blocks):
    row_blocks, col_blocks = blocks.shape
    shaped = values.reshape(row_blocks, BS, col_blocks, BS) * blocks[:, None, :, None]
    return shaped.reshape(row_blocks * BS, col_blocks * BS)


def xor_permute(x, axis, size, s):
    return lax.ppermute(x, axis, perm=[(i, i ^ s) for i in range(size)])


def exchange(xb, n_row, n_col):
    chips = n_col // 2
    same = {0: xb}
    for s in sorted(range(2, chips, 2), reverse=True) + [1]:
        same[s] = xor_permute(xb, "col", n_col, 2 * s)
    col_pieces = [xb]
    for t in range(1, n_row):
        low = t & -t
        col_pieces.append(xor_permute(col_pieces[t ^ low], "row", n_row, low))
    first = sorted(same)
    relay_first = xor_permute(jnp.stack([same[s] for s in first]), "col", n_col, 1)
    other = {}
    for i, s in enumerate(first):
        other[s] = relay_first[i]
    forward = list(range(2, chips, 2))
    if forward:
        sent = xor_permute(jnp.stack([same[s] for s in forward]), "col", n_col, 2)
        relay_sent = xor_permute(sent, "col", n_col, 1)
        for i, s in enumerate(forward):
            same[s ^ 1] = sent[i]
            other[s ^ 1] = relay_sent[i]
    row_pieces = []
    for s in range(chips):
        row_pieces.append(same[s])
        row_pieces.append(other[s])
    return row_pieces, jnp.stack(col_pieces)


def ordered_k_blocks(col_pieces, me_row, me_col, n_col):
    n_row, rows, cols = col_pieces.shape
    per = rows // cols
    split = col_pieces.reshape(n_row * per, cols, cols)
    s = lax.iota(jnp.int32, n_col)
    owner = jnp.bitwise_xor(s, me_col)
    index = jnp.bitwise_xor(owner // per, me_row) * per + owner % per
    return jnp.take(split, index, axis=0)


def contract(row_pieces, k_blocks):
    total = None
    for s, piece in enumerate(row_pieces):
        part = jnp.dot(piece, k_blocks[s], preferred_element_type=jnp.float32)
        total = part if total is None else total + part
    return total


def on_device(density, pattern):
    rows, cols = density.shape
    row_blocks = rows // BS
    col_blocks = cols // BS
    n_row = lax.axis_size("row")
    n_col = lax.axis_size("col")
    me_row = lax.axis_index("row")
    me_col = lax.axis_index("col")
    allowed = allowed_blocks(pattern)
    blocks = lax.dynamic_slice(
        allowed, (me_row * row_blocks, me_col * col_blocks), (row_blocks, col_blocks)
    ).astype(jnp.float32)
    current = apply_mask(density, blocks)
    for step in range(STEPS):
        xb = current.astype(jnp.bfloat16)
        x_row, x_col = exchange(xb, n_row, n_col)
        x_k = ordered_k_blocks(x_col, me_row, me_col, n_col)
        square = apply_mask(contract(x_row, x_k), blocks)
        qb = square.astype(jnp.bfloat16)
        q_row, q_col = exchange(qb, n_row, n_col)
        q_k = ordered_k_blocks(q_col, me_row, me_col, n_col)
        jordan = contract(q_row, x_k) + contract(x_row, q_k)
        current = apply_mask(3.0 * square - jordan, blocks)
    return current


def solution(mesh):
    placed = (P("row", "col"), P())
    return jax.shard_map(
        on_device, mesh=mesh, in_specs=placed, out_specs=P("row", "col"), check_vma=False
    )
```

```python
import jax
import jax.numpy as jnp
from jax import lax
from jax.sharding import PartitionSpec as P

BS = 128
STEPS = 2


def allowed_blocks(pattern):
    count = pattern.shape[0]
    index = lax.iota(jnp.int32, count)
    eye = (index[:, None] == index[None, :]).astype(jnp.int32)
    return jnp.maximum(jnp.maximum(pattern, pattern.T), eye)


def apply_mask(values, blocks):
    row_blocks, col_blocks = blocks.shape
    shaped = values.reshape(row_blocks, BS, col_blocks, BS) * blocks[:, None, :, None]
    return shaped.reshape(row_blocks * BS, col_blocks * BS)


def xor_permute(x, axis, size, s):
    return lax.ppermute(x, axis, perm=[(i, i ^ s) for i in range(size)])


def exchange(xb, n_row, n_col):
    chips = n_col // 2
    same = {0: xb}
    for s in sorted(range(2, chips, 2), reverse=True) + [1]:
        same[s] = xor_permute(xb, "col", n_col, 2 * s)
    col_pieces = [xb] + [xor_permute(xb, "row", n_row, t) for t in range(1, n_row)]
    forward = list(range(2, chips, 2))
    early = [0, 1]
    other = {}
    relay_early = xor_permute(jnp.stack([same[s] for s in early]), "col", n_col, 1)
    for i, s in enumerate(early):
        other[s] = relay_early[i]
    if forward:
        relay_late = xor_permute(jnp.stack([same[s] for s in forward]), "col", n_col, 1)
        for i, s in enumerate(forward):
            other[s] = relay_late[i]
    if forward:
        sent = xor_permute(jnp.stack([same[s] for s in forward]), "col", n_col, 2)
        relay_sent = xor_permute(sent, "col", n_col, 1)
        for i, s in enumerate(forward):
            same[s ^ 1] = sent[i]
            other[s ^ 1] = relay_sent[i]
    row_pieces = []
    for s in range(chips):
        row_pieces.append(same[s])
        row_pieces.append(other[s])
    return row_pieces, jnp.stack(col_pieces)


def ordered_k_blocks(col_pieces, me_row, me_col, n_col):
    n_row, rows, cols = col_pieces.shape
    per = rows // cols
    split = col_pieces.reshape(n_row * per, cols, cols)
    s = lax.iota(jnp.int32, n_col)
    owner = jnp.bitwise_xor(s, me_col)
    index = jnp.bitwise_xor(owner // per, me_row) * per + owner % per
    return jnp.take(split, index, axis=0)


def contract(row_pieces, k_blocks):
    total = None
    for s, piece in enumerate(row_pieces):
        part = jnp.dot(piece, k_blocks[s], preferred_element_type=jnp.float32)
        total = part if total is None else total + part
    return total


def on_device(density, pattern):
    rows, cols = density.shape
    row_blocks = rows // BS
    col_blocks = cols // BS
    n_row = lax.axis_size("row")
    n_col = lax.axis_size("col")
    me_row = lax.axis_index("row")
    me_col = lax.axis_index("col")
    allowed = allowed_blocks(pattern)
    blocks = lax.dynamic_slice(
        allowed, (me_row * row_blocks, me_col * col_blocks), (row_blocks, col_blocks)
    ).astype(jnp.float32)
    current = apply_mask(density, blocks)
    for step in range(STEPS):
        xb = current.astype(jnp.bfloat16)
        x_row, x_col = exchange(xb, n_row, n_col)
        x_k = ordered_k_blocks(x_col, me_row, me_col, n_col)
        square = apply_mask(contract(x_row, x_k), blocks)
        qb = square.astype(jnp.bfloat16)
        q_row, q_col = exchange(qb, n_row, n_col)
        q_k = ordered_k_blocks(q_col, me_row, me_col, n_col)
        jordan = contract(q_row, x_k) + contract(x_row, q_k)
        current = apply_mask(3.0 * square - jordan, blocks)
    return current


def solution(mesh):
    placed = (P("row", "col"), P())
    return jax.shard_map(
        on_device, mesh=mesh, in_specs=placed, out_specs=P("row", "col"), check_vma=False
    )
```

```python
import jax
import jax.numpy as jnp
from jax import lax
from jax.sharding import PartitionSpec as P

BS = 128
STEPS = 2


def allowed_blocks(pattern):
    count = pattern.shape[0]
    index = lax.iota(jnp.int32, count)
    eye = (index[:, None] == index[None, :]).astype(jnp.int32)
    return jnp.maximum(jnp.maximum(pattern, pattern.T), eye)


def apply_mask(values, blocks):
    row_blocks, col_blocks = blocks.shape
    shaped = values.reshape(row_blocks, BS, col_blocks, BS) * blocks[:, None, :, None]
    return shaped.reshape(row_blocks * BS, col_blocks * BS)


def xor_permute(x, axis, size, s):
    return lax.ppermute(x, axis, perm=[(i, i ^ s) for i in range(size)])


def exchange(xb, n_row, n_col):
    chips = n_col // 2
    same = {0: xb}
    for s in sorted(range(2, chips, 2), reverse=True) + [1]:
        same[s] = xor_permute(xb, "col", n_col, 2 * s)
    col_pieces = [xb] + [xor_permute(xb, "row", n_row, t) for t in range(1, n_row) if t & (t - 1) == 0]
    forward = list(range(2, chips, 2))
    if forward:
        later, same[forward[0]] = lax.optimization_barrier((xb, same[forward[0]]))
    else:
        later = xb
    for t in range(3, n_row):
        if t & (t - 1):
            col_pieces.insert(t, xor_permute(later, "row", n_row, t))
    first = sorted(same)
    relay_first = xor_permute(jnp.stack([same[s] for s in first]), "col", n_col, 1)
    other = {}
    for i, s in enumerate(first):
        other[s] = relay_first[i]
    if forward:
        sent = xor_permute(jnp.stack([same[s] for s in forward]), "col", n_col, 2)
        relay_sent = xor_permute(sent, "col", n_col, 1)
        for i, s in enumerate(forward):
            same[s ^ 1] = sent[i]
            other[s ^ 1] = relay_sent[i]
    row_pieces = []
    for s in range(chips):
        row_pieces.append(same[s])
        row_pieces.append(other[s])
    return row_pieces, jnp.stack(col_pieces)


def ordered_k_blocks(col_pieces, me_row, me_col, n_col):
    n_row, rows, cols = col_pieces.shape
    per = rows // cols
    split = col_pieces.reshape(n_row * per, cols, cols)
    s = lax.iota(jnp.int32, n_col)
    owner = jnp.bitwise_xor(s, me_col)
    index = jnp.bitwise_xor(owner // per, me_row) * per + owner % per
    return jnp.take(split, index, axis=0)


def contract(row_pieces, k_blocks):
    total = None
    for s, piece in enumerate(row_pieces):
        part = jnp.dot(piece, k_blocks[s], preferred_element_type=jnp.float32)
        total = part if total is None else total + part
    return total


def on_device(density, pattern):
    rows, cols = density.shape
    row_blocks = rows // BS
    col_blocks = cols // BS
    n_row = lax.axis_size("row")
    n_col = lax.axis_size("col")
    me_row = lax.axis_index("row")
    me_col = lax.axis_index("col")
    allowed = allowed_blocks(pattern)
    blocks = lax.dynamic_slice(
        allowed, (me_row * row_blocks, me_col * col_blocks), (row_blocks, col_blocks)
    ).astype(jnp.float32)
    current = apply_mask(density, blocks)
    for step in range(STEPS):
        xb = current.astype(jnp.bfloat16)
        x_row, x_col = exchange(xb, n_row, n_col)
        x_k = ordered_k_blocks(x_col, me_row, me_col, n_col)
        square = apply_mask(contract(x_row, x_k), blocks)
        qb = square.astype(jnp.bfloat16)
        q_row, q_col = exchange(qb, n_row, n_col)
        q_k = ordered_k_blocks(q_col, me_row, me_col, n_col)
        jordan = contract(q_row, x_k) + contract(x_row, q_k)
        current = apply_mask(3.0 * square - jordan, blocks)
    return current


def solution(mesh):
    placed = (P("row", "col"), P())
    return jax.shard_map(
        on_device, mesh=mesh, in_specs=placed, out_specs=P("row", "col"), check_vma=False
    )
```

```python
import jax
import jax.numpy as jnp
from jax import lax
from jax.sharding import PartitionSpec as P

BS = 128
STEPS = 2


def allowed_blocks(pattern):
    count = pattern.shape[0]
    index = lax.iota(jnp.int32, count)
    eye = (index[:, None] == index[None, :]).astype(jnp.int32)
    return jnp.maximum(jnp.maximum(pattern, pattern.T), eye)


def apply_mask(values, blocks):
    row_blocks, col_blocks = blocks.shape
    shaped = values.reshape(row_blocks, BS, col_blocks, BS) * blocks[:, None, :, None]
    return shaped.reshape(row_blocks * BS, col_blocks * BS)


def xor_permute(x, axis, size, s):
    return lax.ppermute(x, axis, perm=[(i, i ^ s) for i in range(size)])


def exchange(xb, n_row, n_col):
    chips = n_col // 2
    same = {0: xb}
    for s in sorted(range(2, chips, 2), reverse=True) + [1]:
        same[s] = xor_permute(xb, "col", n_col, 2 * s)
    col_pieces = [xb] + [xor_permute(xb, "row", n_row, t) for t in range(1, n_row) if t & (t - 1) == 0]
    forward = list(range(2, chips, 2))
    later, same[1] = lax.optimization_barrier((xb, same[1]))
    for t in range(3, n_row):
        if t & (t - 1):
            col_pieces.insert(t, xor_permute(later, "row", n_row, t))
    first = sorted(same)
    relay_first = xor_permute(jnp.stack([same[s] for s in first]), "col", n_col, 1)
    other = {}
    for i, s in enumerate(first):
        other[s] = relay_first[i]
    if forward:
        sent = xor_permute(jnp.stack([same[s] for s in forward]), "col", n_col, 2)
        relay_sent = xor_permute(sent, "col", n_col, 1)
        for i, s in enumerate(forward):
            same[s ^ 1] = sent[i]
            other[s ^ 1] = relay_sent[i]
    row_pieces = []
    for s in range(chips):
        row_pieces.append(same[s])
        row_pieces.append(other[s])
    return row_pieces, jnp.stack(col_pieces)


def ordered_k_blocks(col_pieces, me_row, me_col, n_col):
    n_row, rows, cols = col_pieces.shape
    per = rows // cols
    split = col_pieces.reshape(n_row * per, cols, cols)
    s = lax.iota(jnp.int32, n_col)
    owner = jnp.bitwise_xor(s, me_col)
    index = jnp.bitwise_xor(owner // per, me_row) * per + owner % per
    return jnp.take(split, index, axis=0)


def contract(row_pieces, k_blocks):
    total = None
    for s, piece in enumerate(row_pieces):
        part = jnp.dot(piece, k_blocks[s], preferred_element_type=jnp.float32)
        total = part if total is None else total + part
    return total


def on_device(density, pattern):
    rows, cols = density.shape
    row_blocks = rows // BS
    col_blocks = cols // BS
    n_row = lax.axis_size("row")
    n_col = lax.axis_size("col")
    me_row = lax.axis_index("row")
    me_col = lax.axis_index("col")
    allowed = allowed_blocks(pattern)
    blocks = lax.dynamic_slice(
        allowed, (me_row * row_blocks, me_col * col_blocks), (row_blocks, col_blocks)
    ).astype(jnp.float32)
    current = apply_mask(density, blocks)
    for step in range(STEPS):
        xb = current.astype(jnp.bfloat16)
        x_row, x_col = exchange(xb, n_row, n_col)
        x_k = ordered_k_blocks(x_col, me_row, me_col, n_col)
        square = apply_mask(contract(x_row, x_k), blocks)
        qb = square.astype(jnp.bfloat16)
        q_row, q_col = exchange(qb, n_row, n_col)
        q_k = ordered_k_blocks(q_col, me_row, me_col, n_col)
        jordan = contract(q_row, x_k) + contract(x_row, q_k)
        current = apply_mask(3.0 * square - jordan, blocks)
    return current


def solution(mesh):
    placed = (P("row", "col"), P())
    return jax.shard_map(
        on_device, mesh=mesh, in_specs=placed, out_specs=P("row", "col"), check_vma=False
    )
```

```python
import jax
import jax.numpy as jnp
from jax import lax
from jax.sharding import PartitionSpec as P

BS = 128
STEPS = 2


def allowed_blocks(pattern):
    count = pattern.shape[0]
    index = lax.iota(jnp.int32, count)
    eye = (index[:, None] == index[None, :]).astype(jnp.int32)
    return jnp.maximum(jnp.maximum(pattern, pattern.T), eye)


def apply_mask(values, blocks):
    row_blocks, col_blocks = blocks.shape
    shaped = values.reshape(row_blocks, BS, col_blocks, BS) * blocks[:, None, :, None]
    return shaped.reshape(row_blocks * BS, col_blocks * BS)


def xor_permute(x, axis, size, s):
    return lax.ppermute(x, axis, perm=[(i, i ^ s) for i in range(size)])


def exchange(xb, n_row, n_col):
    chips = n_col // 2
    same = {0: xb}
    for s in sorted(range(2, chips, 2), reverse=True) + [1]:
        same[s] = xor_permute(xb, "col", n_col, 2 * s)
    col_pieces = [xb] + [xor_permute(xb, "row", n_row, t) for t in range(1, n_row)]
    first = sorted(same)
    relay_first = xor_permute(tuple(same[s] for s in first), "col", n_col, 1)
    other = {}
    for i, s in enumerate(first):
        other[s] = relay_first[i]
    forward = list(range(2, chips, 2))
    if forward:
        sent = xor_permute(jnp.stack([same[s] for s in forward]), "col", n_col, 2)
        relay_sent = xor_permute(sent, "col", n_col, 1)
        for i, s in enumerate(forward):
            same[s ^ 1] = sent[i]
            other[s ^ 1] = relay_sent[i]
    row_pieces = []
    for s in range(chips):
        row_pieces.append(same[s])
        row_pieces.append(other[s])
    return row_pieces, jnp.stack(col_pieces)


def ordered_k_blocks(col_pieces, me_row, me_col, n_col):
    n_row, rows, cols = col_pieces.shape
    per = rows // cols
    split = col_pieces.reshape(n_row * per, cols, cols)
    s = lax.iota(jnp.int32, n_col)
    owner = jnp.bitwise_xor(s, me_col)
    index = jnp.bitwise_xor(owner // per, me_row) * per + owner % per
    return jnp.take(split, index, axis=0)


def contract(row_pieces, k_blocks):
    total = None
    for s, piece in enumerate(row_pieces):
        part = jnp.dot(piece, k_blocks[s], preferred_element_type=jnp.float32)
        total = part if total is None else total + part
    return total


def on_device(density, pattern):
    rows, cols = density.shape
    row_blocks = rows // BS
    col_blocks = cols // BS
    n_row = lax.axis_size("row")
    n_col = lax.axis_size("col")
    me_row = lax.axis_index("row")
    me_col = lax.axis_index("col")
    allowed = allowed_blocks(pattern)
    blocks = lax.dynamic_slice(
        allowed, (me_row * row_blocks, me_col * col_blocks), (row_blocks, col_blocks)
    ).astype(jnp.float32)
    current = apply_mask(density, blocks)
    for step in range(STEPS):
        xb = current.astype(jnp.bfloat16)
        x_row, x_col = exchange(xb, n_row, n_col)
        x_k = ordered_k_blocks(x_col, me_row, me_col, n_col)
        square = apply_mask(contract(x_row, x_k), blocks)
        qb = square.astype(jnp.bfloat16)
        q_row, q_col = exchange(qb, n_row, n_col)
        q_k = ordered_k_blocks(q_col, me_row, me_col, n_col)
        jordan = contract(q_row, x_k) + contract(x_row, q_k)
        current = apply_mask(3.0 * square - jordan, blocks)
    return current


def solution(mesh):
    placed = (P("row", "col"), P())
    return jax.shard_map(
        on_device, mesh=mesh, in_specs=placed, out_specs=P("row", "col"), check_vma=False
    )
```
